512 devices in a mesh: snap: 4 (over x), space: 128 (over z, y, core).
Axes of the slice: x: 4, y: 8, z: 8, core: 2. Of those that a mesh axis runs over, the one named last changes fastest.
Arguments:
- field_in: bfloat16 [4, 128, 32, 32, 256], P('snap', 'space'), may hold values from -6 to 6
- ocean_mask: int32 [128, 32, 32], P('space'), may hold values 0 or 1
- cotangent: bfloat16 [4, 128, 32, 32, 256], P('snap', 'space'), may hold values from -6 to 6
- w_first: bfloat16 [3, 3, 256, 128], replicated, may hold values from -0.125 to 0.125
- b_first: float32 [128], replicated, may hold values from -3 to 3
- w_second: bfloat16 [3, 3, 128, 256], replicated, may hold values from -0.1875 to 0.1875
- b_second: float32 [256], replicated, may hold values from -3 to 3
Outputs:
- field_out: bfloat16 [4, 128, 32, 32, 256], P('snap', 'space')
- grad_field: bfloat16 [4, 128, 32, 32, 256], P('snap', 'space')
- grad_w_first: float32 [3, 3, 256, 128], P(None, None, 'space')
- grad_w_second: float32 [3, 3, 128, 256], P(None, None, 'space')
- grad_b_first: float32 [128], P('space')
- grad_b_second: float32 [256], P('space')
The draws below stay inside these ranges and needn't reach their ends.
All inputs are finite; a program needn't handle non-finite values. No bound on the sum of `ocean_mask` on one device may be relied on, other than what follows from the above.
Results may differ from the reference program's by a relative error of at most 0.014.
Values may be sent and summed in bfloat16 or wider, within the bound.
No kernel may reach another device: no remote copies, remote signals or barrier semaphores. Data moves between devices by JAX's collectives and lax.ppermute only.
A program may use at most 64 MiB of HBM per device.

```python
import math
import jax
import jax.numpy as jnp
from jax import lax

C = 256
H = 128
DEV_COLS = 4
CY = 32
CX = 32
SNAPS = 4
REGIONS = 128
DEV_ROWS = 32
NY = 1024
NX = 128


def plant(drawn, stream_key, least, top_value):
    spot = [jax.random.randint(jax.random.fold_in(stream_key, axis), (), 0, length) for axis, length in enumerate(drawn.shape)]
    longest = drawn.shape.index(max(drawn.shape))
    beside = spot[:longest] + [(spot[longest] + 1) % drawn.shape[longest]] + spot[longest + 1:]
    return drawn.at[tuple(spot)].set(least).at[tuple(beside)].set(top_value)


def block_scale(key, extent, cuts, low, high):
    gain = 1.0
    for dim, parts in cuts:
        draws = jax.random.uniform(jax.random.fold_in(jax.random.fold_in(key, 6), dim), (parts,), jnp.float32, low / len(cuts), high / len(cuts))
        gain = gain * jnp.repeat(jnp.exp(draws), extent[dim] // parts).reshape((-1,) + (1,) * (len(extent) - 1 - dim))
    return gain


def normal_values(key, extent, spread, bound, split=(), kind=jnp.bfloat16):
    level = block_scale(key, extent, split, -0.22, 0.18) if split else 1.0
    drawn = jax.random.normal(key, extent, jnp.float32) * spread * level
    return jnp.minimum(jnp.maximum(drawn, -bound), bound).astype(kind)


def setup_inputs(seed: int = 0) -> dict:
    keys = jax.random.split(jax.random.key(seed), 8)
    return {
        "field_in": normal_values(keys[0], (SNAPS, REGIONS, CY, CX, C), 1.0, 6.0, ((0, 4), (1, 128))),
        "ocean_mask": plant((jax.random.randint(keys[1], (REGIONS, CY, CX), 0, 4) < 3).astype(jnp.int32), jax.random.fold_in(keys[1], 1), 0, 1),
        "cotangent": normal_values(keys[2], (SNAPS, REGIONS, CY, CX, C), 1.0, 6.0, ((0, 4), (1, 128))),
        "w_first": normal_values(keys[3], (3, 3, C, H), (9 * C) ** -0.5, 0.125),
        "b_first": normal_values(keys[4], (H,), 0.5, 3.0, (), jnp.float32),
        "w_second": normal_values(keys[5], (3, 3, H, C), (9 * H) ** -0.5, 0.1875),
        "b_second": normal_values(keys[6], (C,), 0.5, 3.0, (), jnp.float32),
    }


ROOT_HALF = 0.7071067811865476
INV_ROOT_TWO_PI = 0.3989422804014327

def gelu_value(pre):
    return 0.5 * pre * (1.0 + lax.erf(pre * ROOT_HALF))

def gelu_slope(pre):
    return 0.5 * (1.0 + lax.erf(pre * ROOT_HALF)) + pre * jnp.exp(-0.5 * pre * pre) * INV_ROOT_TWO_PI

def to_grid(blocks):
    placed = jnp.roll(blocks, 1, axis=0)
    trailing = placed.shape[3:]
    shaped = placed.reshape((DEV_ROWS, DEV_COLS, CY, CX) + trailing)
    shaped = jnp.swapaxes(shaped, 1, 2)
    return shaped.reshape((DEV_ROWS * CY, DEV_COLS * CX) + trailing)

def to_blocks(grid):
    trailing = grid.shape[2:]
    shaped = grid.reshape((DEV_ROWS, CY, DEV_COLS, CX) + trailing)
    shaped = jnp.swapaxes(shaped, 1, 2)
    placed = shaped.reshape((REGIONS, CY, CX) + trailing)
    return jnp.roll(placed, -1, axis=0)

def dilated(source, kernel):
    return lax.conv_general_dilated(source.astype(jnp.float32)[None], kernel.astype(jnp.float32), (1, 1), ((2, 2), (2, 2)), rhs_dilation=(2, 2), dimension_numbers=('NHWC', 'HWIO', 'NHWC'), precision=lax.Precision.HIGHEST)[0]

def flipped(kernel):
    return jnp.swapaxes(kernel[::-1, ::-1], 2, 3)

def tap_sums(source, grad_out):
    padded = jnp.pad(source, ((2, 2), (2, 2), (0, 0)))
    span_y = grad_out.shape[0]
    span_x = grad_out.shape[1]
    flat_out = grad_out.reshape(span_y * span_x, grad_out.shape[2])
    tap_rows = []
    for tap_y in range(3):
        tap_line = []
        for tap_x in range(3):
            window = padded[2 * tap_y:2 * tap_y + span_y, 2 * tap_x:2 * tap_x + span_x].reshape(span_y * span_x, source.shape[2])
            tap_line.append(lax.dot_general(window, flat_out, (((0,), (0,)), ((), ())), preferred_element_type=jnp.float32))
        tap_rows.append(jnp.stack(tap_line))
    return jnp.stack(tap_rows)

def reference(field_in, ocean_mask, cotangent, w_first, b_first, w_second, b_second):
    ocean = to_grid(ocean_mask).astype(jnp.float32)[:, :, None]
    scale = 1.0 / math.sqrt(float(SNAPS * NY * NX))
    grad_wa = jnp.zeros((3, 3, C, H), jnp.float32)
    grad_wb = jnp.zeros((3, 3, H, C), jnp.float32)
    grad_ba = jnp.zeros((H,), jnp.float32)
    grad_bb = jnp.zeros((C,), jnp.float32)
    results = []
    gradients = []
    for snap_index in range(SNAPS):
        source = to_grid(field_in[snap_index])
        pre = dilated(source, w_first) + b_first
        hidden = (ocean * gelu_value(pre)).astype(jnp.bfloat16)
        mixed = dilated(hidden, w_second) + b_second
        results.append(to_blocks((source.astype(jnp.float32) + ocean * mixed).astype(jnp.bfloat16)))
        upstream = to_grid(cotangent[snap_index])
        g_mixed = (ocean * upstream.astype(jnp.float32)).astype(jnp.bfloat16)
        g_hidden = dilated(g_mixed, flipped(w_second))
        g_pre = (ocean * g_hidden * gelu_slope(pre)).astype(jnp.bfloat16)
        g_input = (upstream.astype(jnp.float32) + dilated(g_pre, flipped(w_first))).astype(jnp.bfloat16)
        gradients.append(to_blocks(g_input))
        grad_wb = grad_wb + tap_sums(hidden, g_mixed)
        grad_wa = grad_wa + tap_sums(source, g_pre)
        grad_ba = grad_ba + lax.optimization_barrier(jnp.sum(g_pre.astype(jnp.float32), axis=(0, 1)))
        grad_bb = grad_bb + lax.optimization_barrier(jnp.sum(g_mixed.astype(jnp.float32), axis=(0, 1)))
    return (jnp.stack(results), jnp.stack(gradients), grad_wa * scale, grad_wb * scale, grad_ba * scale, grad_bb * scale)
```

```python
import math

import jax
import jax.numpy as jnp
import numpy as np
from jax import lax
from jax.sharding import Mesh
from jax.sharding import PartitionSpec as P

DEV_COLS = 4
HALO = 4
SPACE = ("z", "y", "core")


ROOT_HALF = 0.7071067811865476
INV_ROOT_TWO_PI = 0.3989422804014327


def from_behind(array, axis, by):
    length = lax.axis_size(axis)
    return lax.ppermute(array, axis, [(i, (i + by) % length) for i in range(length)])


def gelu_value(pre):
    return 0.5 * pre * (1.0 + lax.erf(pre * ROOT_HALF))


def gelu_slope(pre):
    return (
        0.5 * (1.0 + lax.erf(pre * ROOT_HALF)) + pre * jnp.exp(-0.5 * pre * pre) * INV_ROOT_TWO_PI
    )


def dilated(padded, kernel):
    return lax.conv_general_dilated(
        padded[None],
        kernel,
        (1, 1),
        "VALID",
        rhs_dilation=(2, 2),
        dimension_numbers=("NHWC", "HWIO", "NHWC"),
        preferred_element_type=jnp.float32,
    )[0]


def flipped(kernel):
    return jnp.swapaxes(kernel[::-1, ::-1], 2, 3)


def tap_sums(padded, grad_out):
    span_y = grad_out.shape[0]
    span_x = grad_out.shape[1]
    flat_out = grad_out.reshape(span_y * span_x, grad_out.shape[2])
    tap_rows = []
    for tap_y in range(3):
        tap_line = []
        for tap_x in range(3):
            window = padded[2 * tap_y : 2 * tap_y + span_y, 2 * tap_x : 2 * tap_x + span_x].reshape(
                span_y * span_x, padded.shape[2]
            )
            tap_line.append(
                lax.dot_general(
                    window, flat_out, (((0,), (0,)), ((), ())), preferred_element_type=jnp.float32
                )
            )
        tap_rows.append(jnp.stack(tap_line))
    return jnp.stack(tap_rows)


def grid_halo(region, width):
    count = lax.axis_size(SPACE)
    position = (lax.axis_index(SPACE) + 1) % count
    column = position % DEV_COLS
    line = position // DEV_COLS
    last_line = count // DEV_COLS - 1
    strips = []
    for offset in (1, -1):
        edge_cells = region[:, -width:] if offset == 1 else region[:, :width]
        arrived = from_behind(edge_cells, SPACE, offset)
        inside = column != 0 if offset == 1 else column != DEV_COLS - 1
        strips.append(jnp.where(inside, arrived, jnp.zeros_like(arrived)))
    widened = jnp.concatenate([strips[0], region, strips[1]], axis=1)
    row_bands = []
    for offset in (DEV_COLS, -DEV_COLS):
        edge_cells = widened[-width:] if offset > 0 else widened[:width]
        arrived = from_behind(edge_cells, SPACE, offset)
        inside = line != 0 if offset > 0 else line != last_line
        row_bands.append(jnp.where(inside, arrived, jnp.zeros_like(arrived)))
    return jnp.concatenate([row_bands[0], widened, row_bands[1]], axis=0)


def swap(value, axis, bit):
    size = lax.axis_size(axis)
    return lax.ppermute(value, axis, [(i, i ^ bit) for i in range(size)])


def halve(block, axis, bit):
    half = block.shape[0] // 2
    upper = (lax.axis_index(axis) // bit) % 2
    keep = lax.dynamic_slice_in_dim(block, upper * half, half, axis=0)
    send = lax.dynamic_slice_in_dim(block, (1 - upper) * half, half, axis=0)
    return keep + swap(send, axis, bit)


def reduce_shards(rows, sizes):
    names = ("z", "y", "core")
    counts = [len(_bits(size)) for size in sizes]
    steps = [("core", b) for b in _bits(sizes[2])]
    steps += [("y", b) for b in _bits(sizes[1])]
    steps += [("z", b) for b in _bits(sizes[0])]
    starts = dict(zip(names, np.cumsum([0] + counts[:-1]).tolist()))
    total = dict(zip(names, counts))
    order = [starts[axis] + total[axis] - 1 - int(math.log2(bit)) for axis, bit in steps]
    width = rows.shape[1]
    block = rows.reshape((2,) * len(order) + (width,))
    block = jnp.transpose(block, order + [len(order)]).reshape(rows.shape)
    for axis, bit in steps:
        block = halve(block, axis, bit)
    snap_size = lax.axis_size("snap")
    bit = 1
    while bit < snap_size:
        block = block + swap(block, "snap", bit)
        bit *= 2
    return block


def _bits(size):
    out = []
    bit = 1
    while bit < size:
        out.append(bit)
        bit *= 2
    return out


def local(sizes, field_in, ocean_mask, cotangent, w_first, b_first, w_second, b_second):
    region = field_in[0, 0]
    upstream = cotangent[0, 0]
    channels = region.shape[-1]
    hidden_channels = w_first.shape[-1]
    ocean = ocean_mask[0].astype(jnp.float32)[:, :, None]
    space_count = lax.axis_size(SPACE)
    total = (
        field_in.shape[0]
        * lax.axis_size("snap")
        * space_count
        * region.shape[0]
        * region.shape[1]
    )
    scale = 1.0 / math.sqrt(float(total))
    g_mixed = (ocean * upstream.astype(jnp.float32)).astype(jnp.bfloat16)
    mask_lanes = jnp.broadcast_to(ocean.astype(jnp.bfloat16), region.shape[:2] + (128,))
    packed = jnp.concatenate([region, g_mixed, mask_lanes], axis=-1)
    wide = grid_halo(packed, HALO)
    source_wide = wide[..., :channels]
    mixed_wide = wide[..., channels : 2 * channels]
    ocean_wide = wide[2:-2, 2:-2, 2 * channels : 2 * channels + 1].astype(jnp.float32)
    source_pad = source_wide[2:-2, 2:-2]
    pre = dilated(source_wide, w_first) + b_first
    hidden = (ocean_wide * gelu_value(pre)).astype(jnp.bfloat16)
    mixed = dilated(hidden, w_second) + b_second
    field_out = (region.astype(jnp.float32) + ocean * mixed).astype(jnp.bfloat16)
    grad_wb = tap_sums(hidden, g_mixed)
    grad_bb = jnp.sum(g_mixed.astype(jnp.float32), axis=(0, 1))
    g_hidden = dilated(mixed_wide, flipped(w_second))
    g_pre = (ocean_wide * g_hidden * gelu_slope(pre)).astype(jnp.bfloat16)
    g_input = (upstream.astype(jnp.float32) + dilated(g_pre, flipped(w_first))).astype(
        jnp.bfloat16
    )
    g_pre_inner = g_pre[2:-2, 2:-2]
    grad_wa = tap_sums(source_pad, g_pre_inner)
    grad_ba = jnp.sum(g_pre_inner.astype(jnp.float32), axis=(0, 1))
    per_a = channels // space_count
    per_b = hidden_channels // space_count
    rows = jnp.concatenate(
        [
            jnp.moveaxis(grad_wa.reshape(3, 3, space_count, per_a, hidden_channels), 2, 0).reshape(
                space_count, -1
            ),
            jnp.moveaxis(grad_wb.reshape(3, 3, space_count, per_b, channels), 2, 0).reshape(
                space_count, -1
            ),
            grad_ba.reshape(space_count, per_b),
            grad_bb.reshape(space_count, per_a),
        ],
        axis=1,
    )
    width = rows.shape[1]
    padded_width = -(-width // 128) * 128
    rows = jnp.pad(rows, ((0, 0), (0, padded_width - width)))
    mine = reduce_shards(rows, sizes)[0] * scale
    cut_a = 9 * per_a * hidden_channels
    cut_b = cut_a + 9 * per_b * channels
    return (
        field_out[None, None],
        g_input[None, None],
        mine[:cut_a].reshape(3, 3, per_a, hidden_channels),
        mine[cut_a:cut_b].reshape(3, 3, per_b, channels),
        mine[cut_b : cut_b + per_b],
        mine[cut_b + per_b : cut_b + per_b + per_a],
    )


def solution(mesh):
    snap = mesh.shape["snap"]
    space = mesh.shape["space"]
    core_size = 2
    y_size = 8 if space % 16 == 0 else space // core_size
    z_size = space // (core_size * y_size)
    sizes = (z_size, y_size, core_size)
    grid = Mesh(mesh.devices.reshape(snap, z_size, y_size, core_size), ("snap",) + SPACE)
    placed = (
        P("snap", SPACE, None, None, None),
        P(SPACE, None, None),
        P("snap", SPACE, None, None, None),
        P(),
        P(),
        P(),
        P(),
    )

    def run(*args):
        return local(sizes, *args)

    return jax.shard_map(
        run,
        mesh=grid,
        in_specs=placed,
        out_specs=(
            P("snap", SPACE, None, None, None),
            P("snap", SPACE, None, None, None),
            P(None, None, SPACE, None),
            P(None, None, SPACE, None),
            P(SPACE),
            P(SPACE),
        ),
        check_vma=False,
    )
```

```python
import math

import jax
import jax.numpy as jnp
import numpy as np
from jax import lax
from jax.sharding import Mesh
from jax.sharding import PartitionSpec as P

DEV_COLS = 4
HALO = 4
SPACE = ("z", "y", "core")


ROOT_HALF = 0.7071067811865476
INV_ROOT_TWO_PI = 0.3989422804014327


def from_behind(array, axis, by):
    length = lax.axis_size(axis)
    return lax.ppermute(array, axis, [(i, (i + by) % length) for i in range(length)])


def gelu_value(pre):
    return 0.5 * pre * (1.0 + lax.erf(pre * ROOT_HALF))


def gelu_slope(pre):
    return (
        0.5 * (1.0 + lax.erf(pre * ROOT_HALF)) + pre * jnp.exp(-0.5 * pre * pre) * INV_ROOT_TWO_PI
    )


def dilated(padded, kernel):
    return lax.conv_general_dilated(
        padded[None],
        kernel,
        (1, 1),
        "VALID",
        rhs_dilation=(2, 2),
        dimension_numbers=("NHWC", "HWIO", "NHWC"),
        preferred_element_type=jnp.float32,
    )[0]


def flipped(kernel):
    return jnp.swapaxes(kernel[::-1, ::-1], 2, 3)


def tap_sums(padded, grad_out):
    span_y = grad_out.shape[0]
    span_x = grad_out.shape[1]
    flat_out = grad_out.reshape(span_y * span_x, grad_out.shape[2])
    tap_rows = []
    for tap_y in range(3):
        tap_line = []
        for tap_x in range(3):
            window = padded[2 * tap_y : 2 * tap_y + span_y, 2 * tap_x : 2 * tap_x + span_x].reshape(
                span_y * span_x, padded.shape[2]
            )
            tap_line.append(
                lax.dot_general(
                    window, flat_out, (((0,), (0,)), ((), ())), preferred_element_type=jnp.float32
                )
            )
        tap_rows.append(jnp.stack(tap_line))
    return jnp.stack(tap_rows)


def grid_halo(region, width):
    count = lax.axis_size(SPACE)
    position = (lax.axis_index(SPACE) + 1) % count
    column = position % DEV_COLS
    line = position // DEV_COLS
    last_line = count // DEV_COLS - 1
    strips = []
    for offset in (1, -1):
        edge_cells = region[:, -width:] if offset == 1 else region[:, :width]
        arrived = from_behind(edge_cells, SPACE, offset)
        inside = column != 0 if offset == 1 else column != DEV_COLS - 1
        strips.append(jnp.where(inside, arrived, jnp.zeros_like(arrived)))
    widened = jnp.concatenate([strips[0], region, strips[1]], axis=1)
    row_bands = []
    for offset in (DEV_COLS, -DEV_COLS):
        edge_cells = widened[-width:] if offset > 0 else widened[:width]
        arrived = from_behind(edge_cells, SPACE, offset)
        inside = line != 0 if offset > 0 else line != last_line
        row_bands.append(jnp.where(inside, arrived, jnp.zeros_like(arrived)))
    return jnp.concatenate([row_bands[0], widened, row_bands[1]], axis=0)


def swap(value, axis, bit):
    size = lax.axis_size(axis)
    return lax.ppermute(value, axis, [(i, i ^ bit) for i in range(size)])


def to_wire(send, exact):
    rounded = lax.reduce_precision(send[:, :exact], exponent_bits=8, mantissa_bits=7)
    low = (send[:, :exact] - rounded).astype(jnp.bfloat16)
    return jnp.concatenate(
        [rounded.astype(jnp.bfloat16), low, send[:, 2 * exact :].astype(jnp.bfloat16)], axis=1
    )


def from_wire(got, exact):
    got = got.astype(jnp.float32)
    joined = got[:, :exact] + got[:, exact : 2 * exact]
    return jnp.concatenate([joined, jnp.zeros_like(joined), got[:, 2 * exact :]], axis=1)


def halve(block, axis, bit, exact):
    upper = (lax.axis_index(axis) // bit) % 2
    even, odd = block[0::2], block[1::2]
    keep = jnp.where(upper == 0, even, odd)
    send = jnp.where(upper == 0, odd, even)
    return keep + from_wire(swap(to_wire(send, exact), axis, bit), exact)


def reduce_shards(rows, sizes, exact):
    steps = [("core", b) for b in _bits(sizes[2])]
    steps += [("y", b) for b in _bits(sizes[1])]
    steps += [("z", b) for b in _bits(sizes[0])]
    block = rows
    for axis, bit in steps:
        block = halve(block, axis, bit, exact)
    snap_size = lax.axis_size("snap")
    bit = 1
    while bit < snap_size:
        block = block + swap(block, "snap", bit)
        bit *= 2
    return block


def _bits(size):
    out = []
    bit = 1
    while bit < size:
        out.append(bit)
        bit *= 2
    return out


def local(sizes, field_in, ocean_mask, cotangent, w_first, b_first, w_second, b_second):
    region = field_in[0, 0]
    upstream = cotangent[0, 0]
    channels = region.shape[-1]
    hidden_channels = w_first.shape[-1]
    ocean = ocean_mask[0].astype(jnp.float32)[:, :, None]
    space_count = lax.axis_size(SPACE)
    total = (
        field_in.shape[0]
        * lax.axis_size("snap")
        * space_count
        * region.shape[0]
        * region.shape[1]
    )
    scale = 1.0 / math.sqrt(float(total))
    g_mixed = (ocean * upstream.astype(jnp.float32)).astype(jnp.bfloat16)
    mask_lanes = jnp.broadcast_to(ocean.astype(jnp.bfloat16), region.shape[:2] + (128,))
    packed = jnp.concatenate([region, g_mixed, mask_lanes], axis=-1)
    wide = grid_halo(packed, HALO)
    source_wide = wide[..., :channels]
    mixed_wide = wide[..., channels : 2 * channels]
    ocean_wide = wide[2:-2, 2:-2, 2 * channels : 2 * channels + 1].astype(jnp.float32)
    source_pad = source_wide[2:-2, 2:-2]
    pre = dilated(source_wide, w_first) + b_first
    hidden = (ocean_wide * gelu_value(pre)).astype(jnp.bfloat16)
    mixed = dilated(hidden, w_second) + b_second
    field_out = (region.astype(jnp.float32) + ocean * mixed).astype(jnp.bfloat16)
    grad_wb = tap_sums(hidden, g_mixed)
    grad_bb = jnp.sum(g_mixed.astype(jnp.float32), axis=(0, 1))
    g_hidden = dilated(mixed_wide, flipped(w_second))
    g_pre = (ocean_wide * g_hidden * gelu_slope(pre)).astype(jnp.bfloat16)
    g_input = (upstream.astype(jnp.float32) + dilated(g_pre, flipped(w_first))).astype(
        jnp.bfloat16
    )
    g_pre_inner = g_pre[2:-2, 2:-2]
    grad_wa = tap_sums(source_pad, g_pre_inner)
    grad_ba = jnp.sum(g_pre_inner.astype(jnp.float32), axis=(0, 1))
    per_a = channels // space_count
    per_b = hidden_channels // space_count
    exact = per_a + per_b
    rows = jnp.concatenate(
        [
            grad_ba.reshape(space_count, per_b),
            grad_bb.reshape(space_count, per_a),
            jnp.zeros((space_count, exact), jnp.float32),
            jnp.moveaxis(grad_wa.reshape(3, 3, space_count, per_a, hidden_channels), 2, 0).reshape(
                space_count, -1
            ),
            jnp.moveaxis(grad_wb.reshape(3, 3, space_count, per_b, channels), 2, 0).reshape(
                space_count, -1
            ),
        ],
        axis=1,
    )
    width = rows.shape[1]
    padded_width = -(-width // 128) * 128
    rows = jnp.pad(rows, ((0, 0), (0, padded_width - width)))
    mine = reduce_shards(rows, sizes, exact)[0] * scale
    cut_a = 2 * exact + 9 * per_a * hidden_channels
    cut_b = cut_a + 9 * per_b * channels
    return (
        field_out[None, None],
        g_input[None, None],
        mine[2 * exact : cut_a].reshape(3, 3, per_a, hidden_channels),
        mine[cut_a:cut_b].reshape(3, 3, per_b, channels),
        mine[:per_b],
        mine[per_b:exact],
    )


def solution(mesh):
    snap = mesh.shape["snap"]
    space = mesh.shape["space"]
    core_size = 2
    y_size = 8 if space % 16 == 0 else space // core_size
    z_size = space // (core_size * y_size)
    sizes = (z_size, y_size, core_size)
    grid = Mesh(mesh.devices.reshape(snap, z_size, y_size, core_size), ("snap",) + SPACE)
    placed = (
        P("snap", SPACE, None, None, None),
        P(SPACE, None, None),
        P("snap", SPACE, None, None, None),
        P(),
        P(),
        P(),
        P(),
    )

    def run(*args):
        return local(sizes, *args)

    return jax.shard_map(
        run,
        mesh=grid,
        in_specs=placed,
        out_specs=(
            P("snap", SPACE, None, None, None),
            P("snap", SPACE, None, None, None),
            P(None, None, SPACE, None),
            P(None, None, SPACE, None),
            P(SPACE),
            P(SPACE),
        ),
        check_vma=False,
    )
```

```python
import math

import jax
import jax.numpy as jnp
import numpy as np
from jax import lax
from jax.sharding import Mesh
from jax.sharding import PartitionSpec as P

DEV_COLS = 4
HALO = 4
SPACE = ("z", "y", "core")


ROOT_HALF = 0.7071067811865476
INV_ROOT_TWO_PI = 0.3989422804014327


def from_behind(array, axis, by):
    length = lax.axis_size(axis)
    return lax.ppermute(array, axis, [(i, (i + by) % length) for i in range(length)])


def gelu_value(pre):
    return 0.5 * pre * (1.0 + lax.erf(pre * ROOT_HALF))


def gelu_slope(pre):
    return (
        0.5 * (1.0 + lax.erf(pre * ROOT_HALF)) + pre * jnp.exp(-0.5 * pre * pre) * INV_ROOT_TWO_PI
    )


def dilated(padded, kernel):
    return lax.conv_general_dilated(
        padded[None],
        kernel,
        (1, 1),
        "VALID",
        rhs_dilation=(2, 2),
        dimension_numbers=("NHWC", "HWIO", "NHWC"),
        preferred_element_type=jnp.float32,
    )[0]


def flipped(kernel):
    return jnp.swapaxes(kernel[::-1, ::-1], 2, 3)


def tap_sums(padded, grad_out):
    span_y = grad_out.shape[0]
    span_x = grad_out.shape[1]
    flat_out = grad_out.reshape(span_y * span_x, grad_out.shape[2])
    tap_rows = []
    for tap_y in range(3):
        tap_line = []
        for tap_x in range(3):
            window = padded[2 * tap_y : 2 * tap_y + span_y, 2 * tap_x : 2 * tap_x + span_x].reshape(
                span_y * span_x, padded.shape[2]
            )
            tap_line.append(
                lax.dot_general(
                    window, flat_out, (((0,), (0,)), ((), ())), preferred_element_type=jnp.float32
                )
            )
        tap_rows.append(jnp.stack(tap_line))
    return jnp.stack(tap_rows)


def grid_halo(region, width):
    count = lax.axis_size(SPACE)
    position = (lax.axis_index(SPACE) + 1) % count
    column = position % DEV_COLS
    line = position // DEV_COLS
    last_line = count // DEV_COLS - 1
    strips = []
    for offset in (1, -1):
        edge_cells = region[:, -width:] if offset == 1 else region[:, :width]
        arrived = from_behind(edge_cells, SPACE, offset)
        inside = column != 0 if offset == 1 else column != DEV_COLS - 1
        strips.append(jnp.where(inside, arrived, jnp.zeros_like(arrived)))
    widened = jnp.concatenate([strips[0], region, strips[1]], axis=1)
    row_bands = []
    for offset in (DEV_COLS, -DEV_COLS):
        edge_cells = widened[-width:] if offset > 0 else widened[:width]
        arrived = from_behind(edge_cells, SPACE, offset)
        inside = line != 0 if offset > 0 else line != last_line
        row_bands.append(jnp.where(inside, arrived, jnp.zeros_like(arrived)))
    return jnp.concatenate([row_bands[0], widened, row_bands[1]], axis=0)


def swap(value, axis, bit):
    size = lax.axis_size(axis)
    return lax.ppermute(value, axis, [(i, i ^ bit) for i in range(size)])


def halve(block, axis, bit):
    half = block.shape[0] // 2
    upper = (lax.axis_index(axis) // bit) % 2
    keep = lax.dynamic_slice_in_dim(block, upper * half, half, axis=0)
    send = lax.dynamic_slice_in_dim(block, (1 - upper) * half, half, axis=0)
    return keep + swap(send, axis, bit)


def butterfly_steps(sizes):
    steps = [("core", b) for b in _bits(sizes[2])]
    steps += [("y", b) for b in _bits(sizes[1])]
    steps += [("z", b) for b in _bits(sizes[0])]
    return steps


def shard_bit_order(sizes):
    names = ("z", "y", "core")
    counts = [len(_bits(size)) for size in sizes]
    starts = dict(zip(names, np.cumsum([0] + counts[:-1]).tolist()))
    total = dict(zip(names, counts))
    return [
        starts[axis] + total[axis] - 1 - int(math.log2(bit)) for axis, bit in butterfly_steps(sizes)
    ]


def reduce_shards(block, sizes):
    for axis, bit in butterfly_steps(sizes):
        block = halve(block, axis, bit)
    snap_size = lax.axis_size("snap")
    bit = 1
    while bit < snap_size:
        block = block + swap(block, "snap", bit)
        bit *= 2
    return block


def shard_rows(grad, sizes, per):
    order = shard_bit_order(sizes)
    bits = len(order)
    split = grad.reshape((9,) + (2,) * bits + (per * grad.shape[-1],))
    moved = jnp.transpose(split, [1 + o for o in order] + [0, bits + 1])
    return moved.reshape(2**bits, -1)


def bias_rows(grad, sizes, per):
    order = shard_bit_order(sizes)
    split = grad.reshape((2,) * len(order) + (per,))
    return jnp.transpose(split, order + [len(order)]).reshape(2 ** len(order), per)


def _bits(size):
    out = []
    bit = 1
    while bit < size:
        out.append(bit)
        bit *= 2
    return out


def local(sizes, field_in, ocean_mask, cotangent, w_first, b_first, w_second, b_second):
    region = field_in[0, 0]
    upstream = cotangent[0, 0]
    channels = region.shape[-1]
    hidden_channels = w_first.shape[-1]
    ocean = ocean_mask[0].astype(jnp.float32)[:, :, None]
    space_count = lax.axis_size(SPACE)
    total = (
        field_in.shape[0]
        * lax.axis_size("snap")
        * space_count
        * region.shape[0]
        * region.shape[1]
    )
    scale = 1.0 / math.sqrt(float(total))
    g_mixed = (ocean * upstream.astype(jnp.float32)).astype(jnp.bfloat16)
    mask_lanes = jnp.broadcast_to(ocean.astype(jnp.bfloat16), region.shape[:2] + (128,))
    packed = jnp.concatenate([region, g_mixed, mask_lanes], axis=-1)
    wide = grid_halo(packed, HALO)
    source_wide = wide[..., :channels]
    mixed_wide = wide[..., channels : 2 * channels]
    ocean_wide = wide[2:-2, 2:-2, 2 * channels : 2 * channels + 1].astype(jnp.float32)
    source_pad = source_wide[2:-2, 2:-2]
    pre = dilated(source_wide, w_first) + b_first
    hidden = (ocean_wide * gelu_value(pre)).astype(jnp.bfloat16)
    mixed = dilated(hidden, w_second) + b_second
    field_out = (region.astype(jnp.float32) + ocean * mixed).astype(jnp.bfloat16)
    grad_wb = tap_sums(hidden, g_mixed)
    grad_bb = jnp.sum(g_mixed.astype(jnp.float32), axis=(0, 1))
    g_hidden = dilated(mixed_wide, flipped(w_second))
    g_pre = (ocean_wide * g_hidden * gelu_slope(pre)).astype(jnp.bfloat16)
    g_input = (upstream.astype(jnp.float32) + dilated(g_pre, flipped(w_first))).astype(
        jnp.bfloat16
    )
    g_pre_inner = g_pre[2:-2, 2:-2]
    grad_wa = tap_sums(source_pad, g_pre_inner)
    grad_ba = jnp.sum(g_pre_inner.astype(jnp.float32), axis=(0, 1))
    per_a = channels // space_count
    per_b = hidden_channels // space_count
    rows = jnp.concatenate(
        [
            shard_rows(grad_wa, sizes, per_a),
            shard_rows(grad_wb, sizes, per_b),
            bias_rows(grad_ba, sizes, per_b),
            bias_rows(grad_bb, sizes, per_a),
        ],
        axis=1,
    )
    width = rows.shape[1]
    padded_width = -(-width // 128) * 128
    rows = jnp.pad(rows, ((0, 0), (0, padded_width - width)))
    mine = reduce_shards(rows, sizes)[0] * scale
    cut_a = 9 * per_a * hidden_channels
    cut_b = cut_a + 9 * per_b * channels
    return (
        field_out[None, None],
        g_input[None, None],
        mine[:cut_a].reshape(3, 3, per_a, hidden_channels),
        mine[cut_a:cut_b].reshape(3, 3, per_b, channels),
        mine[cut_b : cut_b + per_b],
        mine[cut_b + per_b : cut_b + per_b + per_a],
    )


def solution(mesh):
    snap = mesh.shape["snap"]
    space = mesh.shape["space"]
    core_size = 2
    y_size = 8 if space % 16 == 0 else space // core_size
    z_size = space // (core_size * y_size)
    sizes = (z_size, y_size, core_size)
    grid = Mesh(mesh.devices.reshape(snap, z_size, y_size, core_size), ("snap",) + SPACE)
    placed = (
        P("snap", SPACE, None, None, None),
        P(SPACE, None, None),
        P("snap", SPACE, None, None, None),
        P(),
        P(),
        P(),
        P(),
    )

    def run(*args):
        return local(sizes, *args)

    return jax.shard_map(
        run,
        mesh=grid,
        in_specs=placed,
        out_specs=(
            P("snap", SPACE, None, None, None),
            P("snap", SPACE, None, None, None),
            P(None, None, SPACE, None),
            P(None, None, SPACE, None),
            P(SPACE),
            P(SPACE),
        ),
        check_vma=False,
    )
```

```python
import math

import jax
import jax.numpy as jnp
import numpy as np
from jax import lax
from jax.sharding import Mesh
from jax.sharding import PartitionSpec as P

DEV_COLS = 4
HALO = 4
SPACE = ("z", "y", "core")


ROOT_HALF = 0.7071067811865476
INV_ROOT_TWO_PI = 0.3989422804014327


def from_behind(array, axis, by):
    length = lax.axis_size(axis)
    return lax.ppermute(array, axis, [(i, (i + by) % length) for i in range(length)])


def gelu_value(pre):
    return 0.5 * pre * (1.0 + lax.erf(pre * ROOT_HALF))


def gelu_slope(pre):
    return (
        0.5 * (1.0 + lax.erf(pre * ROOT_HALF)) + pre * jnp.exp(-0.5 * pre * pre) * INV_ROOT_TWO_PI
    )


def dilated(padded, kernel):
    return lax.conv_general_dilated(
        padded[None],
        kernel,
        (1, 1),
        "VALID",
        rhs_dilation=(2, 2),
        dimension_numbers=("NHWC", "HWIO", "NHWC"),
        preferred_element_type=jnp.float32,
    )[0]


def flipped(kernel):
    return jnp.swapaxes(kernel[::-1, ::-1], 2, 3)


def tap_sums(padded, grad_out):
    span_y = grad_out.shape[0]
    span_x = grad_out.shape[1]
    flat_out = grad_out.reshape(span_y * span_x, grad_out.shape[2])
    tap_rows = []
    for tap_y in range(3):
        tap_line = []
        for tap_x in range(3):
            window = padded[2 * tap_y : 2 * tap_y + span_y, 2 * tap_x : 2 * tap_x + span_x].reshape(
                span_y * span_x, padded.shape[2]
            )
            tap_line.append(
                lax.dot_general(
                    window, flat_out, (((0,), (0,)), ((), ())), preferred_element_type=jnp.float32
                )
            )
        tap_rows.append(jnp.stack(tap_line))
    return jnp.stack(tap_rows)


def grid_halo(region, width):
    count = lax.axis_size(SPACE)
    position = (lax.axis_index(SPACE) + 1) % count
    column = position % DEV_COLS
    line = position // DEV_COLS
    last_line = count // DEV_COLS - 1
    strips = []
    for offset in (1, -1):
        edge_cells = region[:, -width:] if offset == 1 else region[:, :width]
        arrived = from_behind(edge_cells, SPACE, offset)
        inside = column != 0 if offset == 1 else column != DEV_COLS - 1
        strips.append(jnp.where(inside, arrived, jnp.zeros_like(arrived)))
    widened = jnp.concatenate([strips[0], region, strips[1]], axis=1)
    row_bands = []
    for offset in (DEV_COLS, -DEV_COLS):
        edge_cells = widened[-width:] if offset > 0 else widened[:width]
        arrived = from_behind(edge_cells, SPACE, offset)
        inside = line != 0 if offset > 0 else line != last_line
        row_bands.append(jnp.where(inside, arrived, jnp.zeros_like(arrived)))
    return jnp.concatenate([row_bands[0], widened, row_bands[1]], axis=0)


def swap(value, axis, bit):
    size = lax.axis_size(axis)
    return lax.ppermute(value, axis, [(i, i ^ bit) for i in range(size)])


def halve(block, axis, bit):
    half = block.shape[0] // 2
    upper = (lax.axis_index(axis) // bit) % 2
    keep = lax.dynamic_slice_in_dim(block, upper * half, half, axis=0)
    send = lax.dynamic_slice_in_dim(block, (1 - upper) * half, half, axis=0)
    return keep + swap(send, axis, bit)


def butterfly_steps(sizes, z_first):
    core = [("core", b) for b in _bits(sizes[2])]
    y = [("y", b) for b in _bits(sizes[1])]
    z = [("z", b) for b in _bits(sizes[0])]
    return core + (z + y if z_first else y + z)


def shard_bit_order(sizes, z_first):
    names = ("z", "y", "core")
    counts = [len(_bits(size)) for size in sizes]
    starts = dict(zip(names, np.cumsum([0] + counts[:-1]).tolist()))
    total = dict(zip(names, counts))
    return [
        starts[axis] + total[axis] - 1 - int(math.log2(bit))
        for axis, bit in butterfly_steps(sizes, z_first)
    ]


def reduce_shards(blocks, sizes):
    first, second = blocks
    for (axis_a, bit_a), (axis_b, bit_b) in zip(
        butterfly_steps(sizes, False), butterfly_steps(sizes, True)
    ):
        first = halve(first, axis_a, bit_a)
        second = halve(second, axis_b, bit_b)
    block = jnp.concatenate([first, second], axis=1)
    snap_size = lax.axis_size("snap")
    bit = 1
    while bit < snap_size:
        block = block + swap(block, "snap", bit)
        bit *= 2
    return block


def shard_rows(grad, order, per):
    bits = len(order)
    split = grad.reshape((9,) + (2,) * bits + (per * grad.shape[-1],))
    moved = jnp.transpose(split, [1 + o for o in order] + [0, bits + 1])
    return moved.reshape(2**bits, -1)


def bias_rows(grad, order, per):
    split = grad.reshape((2,) * len(order) + (per,))
    return jnp.transpose(split, order + [len(order)]).reshape(2 ** len(order), per)


def lane_pad(rows):
    width = rows.shape[1]
    return jnp.pad(rows, ((0, 0), (0, -(-width // 128) * 128 - width)))


def _bits(size):
    out = []
    bit = 1
    while bit < size:
        out.append(bit)
        bit *= 2
    return out


def local(sizes, field_in, ocean_mask, cotangent, w_first, b_first, w_second, b_second):
    region = field_in[0, 0]
    upstream = cotangent[0, 0]
    channels = region.shape[-1]
    hidden_channels = w_first.shape[-1]
    ocean = ocean_mask[0].astype(jnp.float32)[:, :, None]
    space_count = lax.axis_size(SPACE)
    total = (
        field_in.shape[0]
        * lax.axis_size("snap")
        * space_count
        * region.shape[0]
        * region.shape[1]
    )
    scale = 1.0 / math.sqrt(float(total))
    g_mixed = (ocean * upstream.astype(jnp.float32)).astype(jnp.bfloat16)
    mask_lanes = jnp.broadcast_to(ocean.astype(jnp.bfloat16), region.shape[:2] + (128,))
    packed = jnp.concatenate([region, g_mixed, mask_lanes], axis=-1)
    wide = grid_halo(packed, HALO)
    source_wide = wide[..., :channels]
    mixed_wide = wide[..., channels : 2 * channels]
    ocean_wide = wide[2:-2, 2:-2, 2 * channels : 2 * channels + 1].astype(jnp.float32)
    source_pad = source_wide[2:-2, 2:-2]
    pre = dilated(source_wide, w_first) + b_first
    hidden = (ocean_wide * gelu_value(pre)).astype(jnp.bfloat16)
    mixed = dilated(hidden, w_second) + b_second
    field_out = (region.astype(jnp.float32) + ocean * mixed).astype(jnp.bfloat16)
    grad_wb = tap_sums(hidden, g_mixed)
    grad_bb = jnp.sum(g_mixed.astype(jnp.float32), axis=(0, 1))
    g_hidden = dilated(mixed_wide, flipped(w_second))
    g_pre = (ocean_wide * g_hidden * gelu_slope(pre)).astype(jnp.bfloat16)
    g_input = (upstream.astype(jnp.float32) + dilated(g_pre, flipped(w_first))).astype(
        jnp.bfloat16
    )
    g_pre_inner = g_pre[2:-2, 2:-2]
    grad_wa = tap_sums(source_pad, g_pre_inner)
    grad_ba = jnp.sum(g_pre_inner.astype(jnp.float32), axis=(0, 1))
    per_a = channels // space_count
    per_b = hidden_channels // space_count
    order_a = shard_bit_order(sizes, False)
    order_b = shard_bit_order(sizes, True)
    rows_a = lane_pad(
        jnp.concatenate(
            [shard_rows(grad_wa, order_a, per_a), bias_rows(grad_ba, order_a, per_b)], axis=1
        )
    )
    rows_b = lane_pad(
        jnp.concatenate(
            [shard_rows(grad_wb, order_b, per_b), bias_rows(grad_bb, order_b, per_a)], axis=1
        )
    )
    mine = reduce_shards((rows_a, rows_b), sizes)[0] * scale
    size_a = 9 * per_a * hidden_channels
    size_b = 9 * per_b * channels
    base_b = rows_a.shape[1]
    return (
        field_out[None, None],
        g_input[None, None],
        mine[:size_a].reshape(3, 3, per_a, hidden_channels),
        mine[base_b : base_b + size_b].reshape(3, 3, per_b, channels),
        mine[size_a : size_a + per_b],
        mine[base_b + size_b : base_b + size_b + per_a],
    )


def solution(mesh):
    snap = mesh.shape["snap"]
    space = mesh.shape["space"]
    core_size = 2
    y_size = 8 if space % 16 == 0 else space // core_size
    z_size = space // (core_size * y_size)
    sizes = (z_size, y_size, core_size)
    grid = Mesh(mesh.devices.reshape(snap, z_size, y_size, core_size), ("snap",) + SPACE)
    placed = (
        P("snap", SPACE, None, None, None),
        P(SPACE, None, None),
        P("snap", SPACE, None, None, None),
        P(),
        P(),
        P(),
        P(),
    )

    def run(*args):
        return local(sizes, *args)

    return jax.shard_map(
        run,
        mesh=grid,
        in_specs=placed,
        out_specs=(
            P("snap", SPACE, None, None, None),
            P("snap", SPACE, None, None, None),
            P(None, None, SPACE, None),
            P(None, None, SPACE, None),
            P(SPACE),
            P(SPACE),
        ),
        check_vma=False,
    )
```

```python
import math

import jax
import jax.numpy as jnp
import numpy as np
from jax import lax
from jax.sharding import Mesh
from jax.sharding import PartitionSpec as P

DEV_COLS = 4
HALO = 4
SPACE = ("z", "y", "core")


ROOT_HALF = 0.7071067811865476
INV_ROOT_TWO_PI = 0.3989422804014327


def from_behind(array, axis, by):
    length = lax.axis_size(axis)
    return lax.ppermute(array, axis, [(i, (i + by) % length) for i in range(length)])


def gelu_value(pre):
    return 0.5 * pre * (1.0 + lax.erf(pre * ROOT_HALF))


def gelu_slope(pre):
    return (
        0.5 * (1.0 + lax.erf(pre * ROOT_HALF)) + pre * jnp.exp(-0.5 * pre * pre) * INV_ROOT_TWO_PI
    )


def dilated(padded, kernel):
    return lax.conv_general_dilated(
        padded[None],
        kernel,
        (1, 1),
        "VALID",
        rhs_dilation=(2, 2),
        dimension_numbers=("NHWC", "HWIO", "NHWC"),
        preferred_element_type=jnp.float32,
    )[0]


def flipped(kernel):
    return jnp.swapaxes(kernel[::-1, ::-1], 2, 3)


def tap_sums(padded, grad_out):
    span_y = grad_out.shape[0]
    span_x = grad_out.shape[1]
    flat_out = grad_out.reshape(span_y * span_x, grad_out.shape[2])
    tap_rows = []
    for tap_y in range(3):
        tap_line = []
        for tap_x in range(3):
            window = padded[2 * tap_y : 2 * tap_y + span_y, 2 * tap_x : 2 * tap_x + span_x].reshape(
                span_y * span_x, padded.shape[2]
            )
            tap_line.append(
                lax.dot_general(
                    window, flat_out, (((0,), (0,)), ((), ())), preferred_element_type=jnp.float32
                )
            )
        tap_rows.append(jnp.stack(tap_line))
    return jnp.stack(tap_rows)


def grid_halo(region, width):
    count = lax.axis_size(SPACE)
    position = (lax.axis_index(SPACE) + 1) % count
    column = position % DEV_COLS
    line = position // DEV_COLS
    lines = count // DEV_COLS
    rows_of = {-1: slice(-width, None), 0: slice(None), 1: slice(0, width)}
    bands = []
    for d_line in (-1, 0, 1):
        band = []
        for d_col in (-1, 0, 1):
            if d_line == 0 and d_col == 0:
                band.append(region)
                continue
            cells = region[rows_of[d_line], rows_of[d_col]]
            arrived = from_behind(cells, SPACE, -(DEV_COLS * d_line + d_col))
            inside = (
                (line + d_line >= 0)
                & (line + d_line < lines)
                & (column + d_col >= 0)
                & (column + d_col < DEV_COLS)
            )
            band.append(jnp.where(inside, arrived, jnp.zeros_like(arrived)))
        bands.append(jnp.concatenate(band, axis=1))
    return jnp.concatenate(bands, axis=0)


def swap(value, axis, bit):
    size = lax.axis_size(axis)
    return lax.ppermute(value, axis, [(i, i ^ bit) for i in range(size)])


def halve(block, axis, bit):
    half = block.shape[0] // 2
    upper = (lax.axis_index(axis) // bit) % 2
    keep = lax.dynamic_slice_in_dim(block, upper * half, half, axis=0)
    send = lax.dynamic_slice_in_dim(block, (1 - upper) * half, half, axis=0)
    return keep + swap(send, axis, bit)


def butterfly_steps(sizes, z_first):
    core = [("core", b) for b in _bits(sizes[2])]
    y = [("y", b) for b in _bits(sizes[1])]
    z = [("z", b) for b in _bits(sizes[0])]
    return core + (z + y if z_first else y + z)


def shard_bit_order(sizes, z_first):
    names = ("z", "y", "core")
    counts = [len(_bits(size)) for size in sizes]
    starts = dict(zip(names, np.cumsum([0] + counts[:-1]).tolist()))
    total = dict(zip(names, counts))
    return [
        starts[axis] + total[axis] - 1 - int(math.log2(bit))
        for axis, bit in butterfly_steps(sizes, z_first)
    ]


def reduce_shards(blocks, sizes):
    first, second = blocks
    for (axis_a, bit_a), (axis_b, bit_b) in zip(
        butterfly_steps(sizes, False), butterfly_steps(sizes, True)
    ):
        first = halve(first, axis_a, bit_a)
        second = halve(second, axis_b, bit_b)
    block = jnp.concatenate([first, second], axis=1)
    snap_size = lax.axis_size("snap")
    bit = 1
    while bit < snap_size:
        block = block + swap(block, "snap", bit)
        bit *= 2
    return block


def shard_rows(grad, order, per):
    bits = len(order)
    split = grad.reshape((9,) + (2,) * bits + (per * grad.shape[-1],))
    moved = jnp.transpose(split, [1 + o for o in order] + [0, bits + 1])
    return moved.reshape(2**bits, -1)


def bias_rows(grad, order, per):
    split = grad.reshape((2,) * len(order) + (per,))
    return jnp.transpose(split, order + [len(order)]).reshape(2 ** len(order), per)


def lane_pad(rows):
    width = rows.shape[1]
    return jnp.pad(rows, ((0, 0), (0, -(-width // 128) * 128 - width)))


def _bits(size):
    out = []
    bit = 1
    while bit < size:
        out.append(bit)
        bit *= 2
    return out


def local(sizes, field_in, ocean_mask, cotangent, w_first, b_first, w_second, b_second):
    region = field_in[0, 0]
    upstream = cotangent[0, 0]
    channels = region.shape[-1]
    hidden_channels = w_first.shape[-1]
    ocean = ocean_mask[0].astype(jnp.float32)[:, :, None]
    space_count = lax.axis_size(SPACE)
    total = (
        field_in.shape[0]
        * lax.axis_size("snap")
        * space_count
        * region.shape[0]
        * region.shape[1]
    )
    scale = 1.0 / math.sqrt(float(total))
    g_mixed = (ocean * upstream.astype(jnp.float32)).astype(jnp.bfloat16)
    mask_lanes = jnp.broadcast_to(ocean.astype(jnp.bfloat16), region.shape[:2] + (128,))
    packed = jnp.concatenate([region, g_mixed, mask_lanes], axis=-1)
    wide = grid_halo(packed, HALO)
    source_wide = wide[..., :channels]
    mixed_wide = wide[..., channels : 2 * channels]
    ocean_wide = wide[2:-2, 2:-2, 2 * channels : 2 * channels + 1].astype(jnp.float32)
    source_pad = source_wide[2:-2, 2:-2]
    pre = dilated(source_wide, w_first) + b_first
    hidden = (ocean_wide * gelu_value(pre)).astype(jnp.bfloat16)
    mixed = dilated(hidden, w_second) + b_second
    field_out = (region.astype(jnp.float32) + ocean * mixed).astype(jnp.bfloat16)
    grad_wb = tap_sums(hidden, g_mixed)
    grad_bb = jnp.sum(g_mixed.astype(jnp.float32), axis=(0, 1))
    g_hidden = dilated(mixed_wide, flipped(w_second))
    g_pre = (ocean_wide * g_hidden * gelu_slope(pre)).astype(jnp.bfloat16)
    g_input = (upstream.astype(jnp.float32) + dilated(g_pre, flipped(w_first))).astype(
        jnp.bfloat16
    )
    g_pre_inner = g_pre[2:-2, 2:-2]
    grad_wa = tap_sums(source_pad, g_pre_inner)
    grad_ba = jnp.sum(g_pre_inner.astype(jnp.float32), axis=(0, 1))
    per_a = channels // space_count
    per_b = hidden_channels // space_count
    order_a = shard_bit_order(sizes, False)
    order_b = shard_bit_order(sizes, True)
    rows_a = lane_pad(
        jnp.concatenate(
            [shard_rows(grad_wa, order_a, per_a), bias_rows(grad_ba, order_a, per_b)], axis=1
        )
    )
    rows_b = lane_pad(
        jnp.concatenate(
            [shard_rows(grad_wb, order_b, per_b), bias_rows(grad_bb, order_b, per_a)], axis=1
        )
    )
    mine = reduce_shards((rows_a, rows_b), sizes)[0] * scale
    size_a = 9 * per_a * hidden_channels
    size_b = 9 * per_b * channels
    base_b = rows_a.shape[1]
    return (
        field_out[None, None],
        g_input[None, None],
        mine[:size_a].reshape(3, 3, per_a, hidden_channels),
        mine[base_b : base_b + size_b].reshape(3, 3, per_b, channels),
        mine[size_a : size_a + per_b],
        mine[base_b + size_b : base_b + size_b + per_a],
    )


def solution(mesh):
    snap = mesh.shape["snap"]
    space = mesh.shape["space"]
    core_size = 2
    y_size = 8 if space % 16 == 0 else space // core_size
    z_size = space // (core_size * y_size)
    sizes = (z_size, y_size, core_size)
    grid = Mesh(mesh.devices.reshape(snap, z_size, y_size, core_size), ("snap",) + SPACE)
    placed = (
        P("snap", SPACE, None, None, None),
        P(SPACE, None, None),
        P("snap", SPACE, None, None, None),
        P(),
        P(),
        P(),
        P(),
    )

    def run(*args):
        return local(sizes, *args)

    return jax.shard_map(
        run,
        mesh=grid,
        in_specs=placed,
        out_specs=(
            P("snap", SPACE, None, None, None),
            P("snap", SPACE, None, None, None),
            P(None, None, SPACE, None),
            P(None, None, SPACE, None),
            P(SPACE),
            P(SPACE),
        ),
        check_vma=False,
    )
```

```python
import math

import jax
import jax.numpy as jnp
import numpy as np
from jax import lax
from jax.sharding import Mesh
from jax.sharding import PartitionSpec as P

DEV_COLS = 4
HALO = 4
SPACE = ("z", "y", "core")


ROOT_HALF = 0.7071067811865476
INV_ROOT_TWO_PI = 0.3989422804014327


def from_behind(array, axis, by):
    length = lax.axis_size(axis)
    return lax.ppermute(array, axis, [(i, (i + by) % length) for i in range(length)])


def gelu_value(pre):
    return 0.5 * pre * (1.0 + lax.erf(pre * ROOT_HALF))


def gelu_slope(pre):
    return (
        0.5 * (1.0 + lax.erf(pre * ROOT_HALF)) + pre * jnp.exp(-0.5 * pre * pre) * INV_ROOT_TWO_PI
    )


def dilated(padded, kernel):
    return lax.conv_general_dilated(
        padded[None],
        kernel,
        (1, 1),
        "VALID",
        rhs_dilation=(2, 2),
        dimension_numbers=("NHWC", "HWIO", "NHWC"),
        preferred_element_type=jnp.float32,
    )[0]


def flipped(kernel):
    return jnp.swapaxes(kernel[::-1, ::-1], 2, 3)


def tap_sums(padded, grad_out):
    span_y = grad_out.shape[0]
    span_x = grad_out.shape[1]
    cells = span_y * span_x
    flat_out = grad_out.reshape(cells, grad_out.shape[2])
    windows = [
        padded[2 * tap_y : 2 * tap_y + span_y, 2 * tap_x : 2 * tap_x + span_x].reshape(
            cells, padded.shape[2]
        )
        for tap_y in range(3)
        for tap_x in range(3)
    ]
    summed = lax.dot_general(
        jnp.concatenate(windows, axis=1),
        flat_out,
        (((0,), (0,)), ((), ())),
        preferred_element_type=jnp.float32,
    )
    return summed.reshape(3, 3, padded.shape[2], grad_out.shape[2])


def grid_halo(region, width):
    count = lax.axis_size(SPACE)
    position = (lax.axis_index(SPACE) + 1) % count
    column = position % DEV_COLS
    line = position // DEV_COLS
    last_line = count // DEV_COLS - 1
    strips = []
    for offset in (1, -1):
        edge_cells = region[:, -width:] if offset == 1 else region[:, :width]
        arrived = from_behind(edge_cells, SPACE, offset)
        inside = column != 0 if offset == 1 else column != DEV_COLS - 1
        strips.append(jnp.where(inside, arrived, jnp.zeros_like(arrived)))
    widened = jnp.concatenate([strips[0], region, strips[1]], axis=1)
    row_bands = []
    for offset in (DEV_COLS, -DEV_COLS):
        edge_cells = widened[-width:] if offset > 0 else widened[:width]
        arrived = from_behind(edge_cells, SPACE, offset)
        inside = line != 0 if offset > 0 else line != last_line
        row_bands.append(jnp.where(inside, arrived, jnp.zeros_like(arrived)))
    return jnp.concatenate([row_bands[0], widened, row_bands[1]], axis=0)


def swap(value, axis, bit):
    size = lax.axis_size(axis)
    return lax.ppermute(value, axis, [(i, i ^ bit) for i in range(size)])


def halve(block, axis, bit):
    half = block.shape[0] // 2
    upper = (lax.axis_index(axis) // bit) % 2
    keep = lax.dynamic_slice_in_dim(block, upper * half, half, axis=0)
    send = lax.dynamic_slice_in_dim(block, (1 - upper) * half, half, axis=0)
    return keep + swap(send, axis, bit)


def butterfly_steps(sizes, z_first):
    core = [("core", b) for b in _bits(sizes[2])]
    y = [("y", b) for b in _bits(sizes[1])]
    z = [("z", b) for b in _bits(sizes[0])]
    return core + (z + y if z_first else y + z)


def shard_bit_order(sizes, z_first):
    names = ("z", "y", "core")
    counts = [len(_bits(size)) for size in sizes]
    starts = dict(zip(names, np.cumsum([0] + counts[:-1]).tolist()))
    total = dict(zip(names, counts))
    return [
        starts[axis] + total[axis] - 1 - int(math.log2(bit))
        for axis, bit in butterfly_steps(sizes, z_first)
    ]


def reduce_shards(blocks, sizes):
    first, second = blocks
    for (axis_a, bit_a), (axis_b, bit_b) in zip(
        butterfly_steps(sizes, False), butterfly_steps(sizes, True)
    ):
        first = halve(first, axis_a, bit_a)
        second = halve(second, axis_b, bit_b)
    block = jnp.concatenate([first, second], axis=1)
    snap_size = lax.axis_size("snap")
    bit = 1
    while bit < snap_size:
        block = block + swap(block, "snap", bit)
        bit *= 2
    return block


def shard_rows(grad, order, per):
    bits = len(order)
    split = grad.reshape((9,) + (2,) * bits + (per * grad.shape[-1],))
    moved = jnp.transpose(split, [1 + o for o in order] + [0, bits + 1])
    return moved.reshape(2**bits, -1)


def bias_rows(grad, order, per):
    split = grad.reshape((2,) * len(order) + (per,))
    return jnp.transpose(split, order + [len(order)]).reshape(2 ** len(order), per)


def lane_pad(rows):
    width = rows.shape[1]
    return jnp.pad(rows, ((0, 0), (0, -(-width // 128) * 128 - width)))


def _bits(size):
    out = []
    bit = 1
    while bit < size:
        out.append(bit)
        bit *= 2
    return out


def local(sizes, field_in, ocean_mask, cotangent, w_first, b_first, w_second, b_second):
    region = field_in[0, 0]
    upstream = cotangent[0, 0]
    channels = region.shape[-1]
    hidden_channels = w_first.shape[-1]
    ocean = ocean_mask[0].astype(jnp.float32)[:, :, None]
    space_count = lax.axis_size(SPACE)
    total = (
        field_in.shape[0]
        * lax.axis_size("snap")
        * space_count
        * region.shape[0]
        * region.shape[1]
    )
    scale = 1.0 / math.sqrt(float(total))
    g_mixed = (ocean * upstream.astype(jnp.float32)).astype(jnp.bfloat16)
    mask_lanes = jnp.broadcast_to(ocean.astype(jnp.bfloat16), region.shape[:2] + (128,))
    packed = jnp.concatenate([region, g_mixed, mask_lanes], axis=-1)
    wide = grid_halo(packed, HALO)
    source_wide = wide[..., :channels]
    mixed_wide = wide[..., channels : 2 * channels]
    ocean_wide = wide[2:-2, 2:-2, 2 * channels : 2 * channels + 1].astype(jnp.float32)
    source_pad = source_wide[2:-2, 2:-2]
    pre = dilated(source_wide, w_first) + b_first
    hidden = (ocean_wide * gelu_value(pre)).astype(jnp.bfloat16)
    mixed = dilated(hidden, w_second) + b_second
    field_out = (region.astype(jnp.float32) + ocean * mixed).astype(jnp.bfloat16)
    grad_wb = tap_sums(hidden, g_mixed)
    grad_bb = jnp.sum(g_mixed.astype(jnp.float32), axis=(0, 1))
    g_hidden = dilated(mixed_wide, flipped(w_second))
    g_pre = (ocean_wide * g_hidden * gelu_slope(pre)).astype(jnp.bfloat16)
    g_input = (upstream.astype(jnp.float32) + dilated(g_pre, flipped(w_first))).astype(
        jnp.bfloat16
    )
    g_pre_inner = g_pre[2:-2, 2:-2]
    grad_wa = tap_sums(source_pad, g_pre_inner)
    grad_ba = jnp.sum(g_pre_inner.astype(jnp.float32), axis=(0, 1))
    per_a = channels // space_count
    per_b = hidden_channels // space_count
    order_a = shard_bit_order(sizes, False)
    order_b = shard_bit_order(sizes, True)
    rows_a = lane_pad(
        jnp.concatenate(
            [shard_rows(grad_wa, order_a, per_a), bias_rows(grad_ba, order_a, per_b)], axis=1
        )
    )
    rows_b = lane_pad(
        jnp.concatenate(
            [shard_rows(grad_wb, order_b, per_b), bias_rows(grad_bb, order_b, per_a)], axis=1
        )
    )
    mine = reduce_shards((rows_a, rows_b), sizes)[0] * scale
    size_a = 9 * per_a * hidden_channels
    size_b = 9 * per_b * channels
    base_b = rows_a.shape[1]
    return (
        field_out[None, None],
        g_input[None, None],
        mine[:size_a].reshape(3, 3, per_a, hidden_channels),
        mine[base_b : base_b + size_b].reshape(3, 3, per_b, channels),
        mine[size_a : size_a + per_b],
        mine[base_b + size_b : base_b + size_b + per_a],
    )


def solution(mesh):
    snap = mesh.shape["snap"]
    space = mesh.shape["space"]
    core_size = 2
    y_size = 8 if space % 16 == 0 else space // core_size
    z_size = space // (core_size * y_size)
    sizes = (z_size, y_size, core_size)
    grid = Mesh(mesh.devices.reshape(snap, z_size, y_size, core_size), ("snap",) + SPACE)
    placed = (
        P("snap", SPACE, None, None, None),
        P(SPACE, None, None),
        P("snap", SPACE, None, None, None),
        P(),
        P(),
        P(),
        P(),
    )

    def run(*args):
        return local(sizes, *args)

    return jax.shard_map(
        run,
        mesh=grid,
        in_specs=placed,
        out_specs=(
            P("snap", SPACE, None, None, None),
            P("snap", SPACE, None, None, None),
            P(None, None, SPACE, None),
            P(None, None, SPACE, None),
            P(SPACE),
            P(SPACE),
        ),
        check_vma=False,
    )
```

```python
import math

import jax
import jax.numpy as jnp
import numpy as np
from jax import lax
from jax.sharding import Mesh
from jax.sharding import PartitionSpec as P

DEV_COLS = 4
HALO = 4
SPACE = ("z", "y", "core")


ROOT_HALF = 0.7071067811865476
INV_ROOT_TWO_PI = 0.3989422804014327


def from_behind(array, axis, by):
    length = lax.axis_size(axis)
    return lax.ppermute(array, axis, [(i, (i + by) % length) for i in range(length)])


def gelu_value(pre):
    return 0.5 * pre * (1.0 + lax.erf(pre * ROOT_HALF))


def gelu_slope(pre):
    return (
        0.5 * (1.0 + lax.erf(pre * ROOT_HALF)) + pre * jnp.exp(-0.5 * pre * pre) * INV_ROOT_TWO_PI
    )


def dilated(padded, kernel):
    return lax.conv_general_dilated(
        padded[None],
        kernel,
        (1, 1),
        "VALID",
        rhs_dilation=(2, 2),
        dimension_numbers=("NHWC", "HWIO", "NHWC"),
        preferred_element_type=jnp.float32,
    )[0]


def flipped(kernel):
    return jnp.swapaxes(kernel[::-1, ::-1], 2, 3)


def tap_sums(padded, grad_out):
    span_y = grad_out.shape[0]
    span_x = grad_out.shape[1]
    flat_out = grad_out.reshape(span_y * span_x, grad_out.shape[2])
    tap_rows = []
    for tap_y in range(3):
        tap_line = []
        for tap_x in range(3):
            window = padded[2 * tap_y : 2 * tap_y + span_y, 2 * tap_x : 2 * tap_x + span_x].reshape(
                span_y * span_x, padded.shape[2]
            )
            tap_line.append(
                lax.dot_general(
                    window, flat_out, (((0,), (0,)), ((), ())), preferred_element_type=jnp.float32
                )
            )
        tap_rows.append(jnp.stack(tap_line))
    return jnp.stack(tap_rows)


def grid_halo(region, width):
    count = lax.axis_size(SPACE)
    position = (lax.axis_index(SPACE) + 1) % count
    column = position % DEV_COLS
    line = position // DEV_COLS
    last_line = count // DEV_COLS - 1
    strips = []
    for offset in (1, -1):
        edge_cells = region[:, -width:] if offset == 1 else region[:, :width]
        arrived = from_behind(edge_cells, SPACE, offset)
        inside = column != 0 if offset == 1 else column != DEV_COLS - 1
        strips.append(jnp.where(inside, arrived, jnp.zeros_like(arrived)))
    widened = jnp.concatenate([strips[0], region, strips[1]], axis=1)
    row_bands = []
    for offset in (DEV_COLS, -DEV_COLS):
        edge_cells = widened[-width:] if offset > 0 else widened[:width]
        arrived = from_behind(edge_cells, SPACE, offset)
        inside = line != 0 if offset > 0 else line != last_line
        row_bands.append(jnp.where(inside, arrived, jnp.zeros_like(arrived)))
    return jnp.concatenate([row_bands[0], widened, row_bands[1]], axis=0)


def swap(value, axis, bit):
    size = lax.axis_size(axis)
    return lax.ppermute(value, axis, [(i, i ^ bit) for i in range(size)])


def halve(block, axis, bit):
    half = block.shape[0] // 2
    upper = (lax.axis_index(axis) // bit) % 2
    keep = lax.dynamic_slice_in_dim(block, upper * half, half, axis=0)
    send = lax.dynamic_slice_in_dim(block, (1 - upper) * half, half, axis=0)
    return keep + swap(send, axis, bit)


def butterfly_steps(sizes, z_first):
    core = [("core", b) for b in _bits(sizes[2])]
    y = [("y", b) for b in _bits(sizes[1])]
    z = [("z", b) for b in _bits(sizes[0])]
    return core + (z + y if z_first else y + z)


def shard_bit_order(sizes, z_first):
    names = ("z", "y", "core")
    counts = [len(_bits(size)) for size in sizes]
    starts = dict(zip(names, np.cumsum([0] + counts[:-1]).tolist()))
    total = dict(zip(names, counts))
    return [
        starts[axis] + total[axis] - 1 - int(math.log2(bit))
        for axis, bit in butterfly_steps(sizes, z_first)
    ]


def reduce_shards(blocks, sizes):
    first, second = blocks
    shared = 0
    for step_a, step_b in zip(butterfly_steps(sizes, False), butterfly_steps(sizes, True)):
        if step_a != step_b:
            break
        shared += 1
    split = first.shape[1]
    joined = jnp.concatenate([first, second], axis=1)
    for axis, bit in butterfly_steps(sizes, False)[:shared]:
        joined = halve(joined, axis, bit)
    first, second = joined[:, :split], joined[:, split:]
    for (axis_a, bit_a), (axis_b, bit_b) in zip(
        butterfly_steps(sizes, False)[shared:], butterfly_steps(sizes, True)[shared:]
    ):
        first = halve(first, axis_a, bit_a)
        second = halve(second, axis_b, bit_b)
    block = jnp.concatenate([first, second], axis=1)
    snap_size = lax.axis_size("snap")
    bit = 1
    while bit < snap_size:
        block = block + swap(block, "snap", bit)
        bit *= 2
    return block


def shard_rows(grad, order, per):
    bits = len(order)
    split = grad.reshape((9,) + (2,) * bits + (per * grad.shape[-1],))
    moved = jnp.transpose(split, [1 + o for o in order] + [0, bits + 1])
    return moved.reshape(2**bits, -1)


def bias_rows(grad, order, per):
    split = grad.reshape((2,) * len(order) + (per,))
    return jnp.transpose(split, order + [len(order)]).reshape(2 ** len(order), per)


def lane_pad(rows):
    width = rows.shape[1]
    return jnp.pad(rows, ((0, 0), (0, -(-width // 128) * 128 - width)))


def _bits(size):
    out = []
    bit = 1
    while bit < size:
        out.append(bit)
        bit *= 2
    return out


def local(sizes, field_in, ocean_mask, cotangent, w_first, b_first, w_second, b_second):
    region = field_in[0, 0]
    upstream = cotangent[0, 0]
    channels = region.shape[-1]
    hidden_channels = w_first.shape[-1]
    ocean = ocean_mask[0].astype(jnp.float32)[:, :, None]
    space_count = lax.axis_size(SPACE)
    total = (
        field_in.shape[0]
        * lax.axis_size("snap")
        * space_count
        * region.shape[0]
        * region.shape[1]
    )
    scale = 1.0 / math.sqrt(float(total))
    g_mixed = (ocean * upstream.astype(jnp.float32)).astype(jnp.bfloat16)
    mask_lanes = jnp.broadcast_to(ocean.astype(jnp.bfloat16), region.shape[:2] + (128,))
    packed = jnp.concatenate([region, g_mixed, mask_lanes], axis=-1)
    wide = grid_halo(packed, HALO)
    source_wide = wide[..., :channels]
    mixed_wide = wide[..., channels : 2 * channels]
    ocean_wide = wide[2:-2, 2:-2, 2 * channels : 2 * channels + 1].astype(jnp.float32)
    source_pad = source_wide[2:-2, 2:-2]
    pre = dilated(source_wide, w_first) + b_first
    hidden = (ocean_wide * gelu_value(pre)).astype(jnp.bfloat16)
    mixed = dilated(hidden, w_second) + b_second
    field_out = (region.astype(jnp.float32) + ocean * mixed).astype(jnp.bfloat16)
    grad_wb = tap_sums(hidden, g_mixed)
    grad_bb = jnp.sum(g_mixed.astype(jnp.float32), axis=(0, 1))
    g_hidden = dilated(mixed_wide, flipped(w_second))
    g_pre = (ocean_wide * g_hidden * gelu_slope(pre)).astype(jnp.bfloat16)
    g_input = (upstream.astype(jnp.float32) + dilated(g_pre, flipped(w_first))).astype(
        jnp.bfloat16
    )
    g_pre_inner = g_pre[2:-2, 2:-2]
    grad_wa = tap_sums(source_pad, g_pre_inner)
    grad_ba = jnp.sum(g_pre_inner.astype(jnp.float32), axis=(0, 1))
    per_a = channels // space_count
    per_b = hidden_channels // space_count
    order_a = shard_bit_order(sizes, False)
    order_b = shard_bit_order(sizes, True)
    rows_a = lane_pad(
        jnp.concatenate(
            [shard_rows(grad_wa, order_a, per_a), bias_rows(grad_ba, order_a, per_b)], axis=1
        )
    )
    rows_b = lane_pad(
        jnp.concatenate(
            [shard_rows(grad_wb, order_b, per_b), bias_rows(grad_bb, order_b, per_a)], axis=1
        )
    )
    mine = reduce_shards((rows_a, rows_b), sizes)[0] * scale
    size_a = 9 * per_a * hidden_channels
    size_b = 9 * per_b * channels
    base_b = rows_a.shape[1]
    return (
        field_out[None, None],
        g_input[None, None],
        mine[:size_a].reshape(3, 3, per_a, hidden_channels),
        mine[base_b : base_b + size_b].reshape(3, 3, per_b, channels),
        mine[size_a : size_a + per_b],
        mine[base_b + size_b : base_b + size_b + per_a],
    )


def solution(mesh):
    snap = mesh.shape["snap"]
    space = mesh.shape["space"]
    core_size = 2
    y_size = 8 if space % 16 == 0 else space // core_size
    z_size = space // (core_size * y_size)
    sizes = (z_size, y_size, core_size)
    grid = Mesh(mesh.devices.reshape(snap, z_size, y_size, core_size), ("snap",) + SPACE)
    placed = (
        P("snap", SPACE, None, None, None),
        P(SPACE, None, None),
        P("snap", SPACE, None, None, None),
        P(),
        P(),
        P(),
        P(),
    )

    def run(*args):
        return local(sizes, *args)

    return jax.shard_map(
        run,
        mesh=grid,
        in_specs=placed,
        out_specs=(
            P("snap", SPACE, None, None, None),
            P("snap", SPACE, None, None, None),
            P(None, None, SPACE, None),
            P(None, None, SPACE, None),
            P(SPACE),
            P(SPACE),
        ),
        check_vma=False,
    )
```
